32 devices in a mesh: section: 4 (over y, x), expert: 8 (over z, core).
Axes of the slice: x: 2, y: 2, z: 4, core: 2. Of those that a mesh axis runs over, the one named last changes fastest.
Arguments:
- tokens: bfloat16 [4, 2, 256, 2048], P('section', None, 'expert'), may hold values from -6 to 6
- routes: int32 [4, 2, 256, 2], P('section', None, 'expert'), may hold values from 0 to 3, all different within a row; in each aligned block of 32 rows (0 to 31, 32 to 63, ..., all dimensions but the last counted through in order) at most 24 rows name the same one
- combine_weights: float32 [4, 2, 256, 2], P('section', None, 'expert'), may hold values from 0.3 to 1
- norm_gain: float32 [4, 2048], P('section'), may hold values from 0.5 to 1.5
- gate_up: bfloat16 [4, 8, 2048, 768], P('section', 'expert'), may hold values from -0.125 to 0.125
- down: bfloat16 [4, 8, 384, 2048], P('section', 'expert'), may hold values from -0.21875 to 0.21875
Outputs:
- next_inputs: bfloat16 [4, 2, 256, 2048], P('section', None, 'expert')
The draws below stay inside these ranges and needn't reach their ends.
Inputs may be any that keep to these rules, and one draw needn't show every extreme that they name: `routes`: each token names 2 different experts. Among the 32 tokens of one device in one section and micro-batch (aligned blocks of 32 rows) no expert is named more than 24 times.
All inputs are finite; a program needn't handle non-finite values.
Results may differ from the reference program's by a relative error of at most 0.0055.
Values may be sent and summed in bfloat16 or wider, within the bound.
No kernel may reach another device: no remote copies, remote signals or barrier semaphores. Data moves between devices by JAX's collectives and lax.ppermute only.
A program may use at most 64 MiB of HBM per device.

```python
import math
import jax
import jax.numpy as jnp
import numpy as np
from jax import lax

D = 2048
FF = 768
HALF = 384
TOK = 32
MICRO = 2
SECTIONS = 4
EXPERTS = 4
TOPK = 2
CAP = 24
TOKENS = 256
N_EXPERT = 8


def shard_levels(rng, shape, split, least, high):
    level = 1.0
    for dim, shards_of in split:
        draws = jax.random.uniform(jax.random.fold_in(jax.random.fold_in(rng, 6), dim), (shards_of,), jnp.float32, least / len(split), high / len(split))
        level = level * jnp.repeat(jnp.exp(draws), shape[dim] // shards_of).reshape((-1,) + (1,) * (len(shape) - 1 - dim))
    return level


def assign_block(stream_key, own, number, rows, count, top, bound, lean):
    order = jax.random.permutation(stream_key, count)
    packed, ordinary = shares(count, rows * top, bound, lean, True), shares(count, rows * top, bound, lean, False)
    places = jnp.arange(count)

    def named(tallies, rotation):
        used = int((tallies > 0).sum())
        fixed = max(1, used // 4)
        passed = fixed + (places - fixed + rotation * (used - fixed)) % max(1, count - fixed)
        return jnp.zeros((count,), jnp.int32).at[order[jnp.where(places < fixed, places, passed)]].set(jnp.asarray(tallies, jnp.int32))

    tallies = jnp.where(number % 4 == 0, named(packed, number // 4), named(ordinary, number - number // 4 - 1))
    mixed = jax.random.permutation(jax.random.fold_in(own, 3), count)
    source_of, taker = mixed[0:count // 2 * 2:2], mixed[1:count // 2 * 2:2]
    slack = jnp.minimum(tallies[source_of] - 1, bound - tallies[taker]) // 2
    slack = jnp.where((source_of == order[0]) | (taker == order[0]) | (tallies[taker] == 0), 0, jnp.maximum(slack, 0))
    passed = jax.random.randint(jax.random.fold_in(own, 4), (count // 2,), 0, 1 << 20) % (slack + 1)
    tallies = tallies.at[source_of].add(-passed).at[taker].add(passed)
    items = jnp.searchsorted(jnp.cumsum(tallies), jnp.arange(rows * top), side="right").astype(jnp.int32)
    listing = items.reshape(top, rows).T
    listing = listing[jax.random.permutation(jax.random.fold_in(own, 1), rows)]
    rotation = jax.random.randint(jax.random.fold_in(own, 2), (rows, 1), 0, top)
    return jnp.take_along_axis(listing, (jnp.arange(top)[None, :] + rotation) % top, axis=1)


def shares(number_of, total, bound, lean, full):
    weights = [(1 << 20) // math.isqrt(rank ** lean) + 1 for rank in range(1, number_of + 1)]
    largest = bound if full else min(bound, max(-(-total // number_of), total * weights[0] // sum(weights)))
    least = 1 if total - largest >= number_of - 1 else 0
    given, spare = [largest] + [least] * (number_of - 1), total - largest - least * (number_of - 1)
    while spare > 0:
        movable = [i for i in range(1, number_of) if given[i] < largest] or [i for i in range(1, number_of) if given[i] < bound]
        pool, budget = sum([weights[i] for i in movable]), spare
        for i in movable:
            more = min(bound - given[i], max(1, budget * weights[i] // pool), spare)
            given[i] = given[i] + more
            spare = spare - more
    return np.array(given)


def gaussian(stream_key, dims, scale, reach, pieces=(), kind=jnp.bfloat16):
    result = scale * jax.random.normal(stream_key, dims, jnp.float32)
    if pieces:
        result = result * shard_levels(stream_key, dims, pieces, -0.22, 0.18)
    return jnp.clip(result, -reach, reach).astype(kind)


def setup_inputs(seed: int = 0) -> dict:
    splits = jax.random.split(jax.random.key(seed), 7)
    tokens = gaussian(splits[0], (SECTIONS, MICRO, TOKENS, D), 1.0, 6.0, ((0, 4), (2, 8)))
    routes_keys = jax.random.split(jax.random.fold_in(splits[1], 1), SECTIONS * MICRO * TOKENS // TOK)
    routes_turns = jax.random.permutation(jax.random.fold_in(splits[1], 3), SECTIONS * MICRO * TOKENS // TOK)
    routes = jax.vmap(lambda own, number: assign_block(jax.random.fold_in(splits[1], 2), own, number, TOK, EXPERTS, TOPK, CAP, 2))(routes_keys, routes_turns).reshape((SECTIONS, MICRO, TOKENS, TOPK))
    combine_weights = jnp.clip(0.3 + 0.7 * jax.random.uniform(splits[2], (SECTIONS, MICRO, TOKENS, TOPK), jnp.float32) ** shard_levels(splits[2], (SECTIONS, MICRO, TOKENS, TOPK), ((0, 4), (2, 8)), -0.2, 0.2), 0.3, 1.0)
    norm_gain = jnp.clip(1.0 + 0.1 * jax.random.normal(splits[3], (SECTIONS, D), jnp.float32), 0.5, 1.5)
    gate_up = gaussian(splits[4], (SECTIONS, N_EXPERT, D, 2 * HALF), D ** -0.5, 0.125, ((0, 4), (1, 8)))
    down = gaussian(splits[5], (SECTIONS, N_EXPERT, HALF, D), FF ** -0.5, 0.21875, ((0, 4), (1, 8)))
    return {"tokens": tokens, "routes": routes, "combine_weights": combine_weights, "norm_gain": norm_gain, "gate_up": gate_up, "down": down}


EPSILON = 1e-06

def slot_codes(route_block):
    flat = route_block.reshape(-1)
    onehot = (flat[:, None] == jnp.arange(EXPERTS, dtype=jnp.int32)[None, :]).astype(jnp.int32)
    before = jnp.cumsum(onehot, axis=0) - onehot
    slot = lax.optimization_barrier(jnp.sum(before * onehot, axis=1)).astype(jnp.int32)
    return (flat * CAP + slot).astype(jnp.int32).reshape(route_block.shape)

def normalize(block, gain):
    values = block.astype(jnp.float32)
    scale = lax.rsqrt(lax.optimization_barrier(jnp.mean(values * values, axis=-1, keepdims=True)) + EPSILON)
    return (values * scale * gain).astype(jnp.bfloat16)

def expert_half(token_rows, weights_gu, weights_dn):
    joined = jnp.dot(token_rows, weights_gu, preferred_element_type=jnp.float32)
    gate = joined[:, :HALF]
    upward = joined[:, HALF:]
    hidden = (jax.nn.silu(gate) * upward).astype(jnp.bfloat16)
    return jnp.dot(hidden, weights_dn, preferred_element_type=jnp.float32).astype(jnp.bfloat16)

def run_expert(operands):
    buffer, pair_gu, pair_dn = operands
    first = expert_half(buffer, pair_gu[0], pair_dn[0])
    second = expert_half(buffer, pair_gu[1], pair_dn[1])
    return (first.astype(jnp.float32) + second.astype(jnp.float32)).astype(jnp.bfloat16)

def one_section(operands):
    section_tokens, section_routes, section_comb, gain, section_gu, section_dn = operands
    pair_gu = section_gu.reshape(EXPERTS, 2, D, 2 * HALF)
    pair_dn = section_dn.reshape(EXPERTS, 2, HALF, D)
    results = []
    for position in range(MICRO):
        inputs = section_tokens[position]
        normed = normalize(inputs, gain)
        codes = jax.vmap(slot_codes)(section_routes[position].reshape(N_EXPERT, TOK, TOPK))
        device = jnp.arange(N_EXPERT, dtype=jnp.int32)[:, None, None]
        expert = (codes // CAP).astype(jnp.int32)
        place = (device * CAP + codes % CAP).astype(jnp.int32)
        values = jnp.broadcast_to(normed.reshape(N_EXPERT, TOK, 1, D), (N_EXPERT, TOK, TOPK, D))
        buffer = jnp.zeros((EXPERTS, N_EXPERT * CAP, D), jnp.bfloat16).at[expert, place].set(values)
        outputs = lax.map(run_expert, (buffer, pair_gu, pair_dn))
        picked = outputs[expert, place].astype(jnp.float32)
        weights = section_comb[position].reshape(N_EXPERT, TOK, TOPK)
        mixed = inputs.astype(jnp.float32).reshape(N_EXPERT, TOK, D) + lax.optimization_barrier(jnp.sum(weights[..., None] * picked, axis=2))
        results.append(mixed.reshape(TOKENS, D).astype(jnp.bfloat16))
    return jnp.stack(results)

def reference(tokens, routes, combine_weights, norm_gain, gate_up, down):
    layers = lax.map(one_section, (tokens, routes, combine_weights, norm_gain, gate_up, down))
    return jnp.roll(layers, 1, axis=0)
```

```python
import jax
import jax.numpy as jnp
from jax import lax
from jax.sharding import PartitionSpec as P

EPSILON = 1e-06


def from_behind(value, axis, steps):
    count = lax.axis_size(axis)
    pairs = [(source, (source + steps) % count) for source in range(count)]
    return lax.ppermute(value, axis, pairs)


def normalize(block, gain):
    values = block.astype(jnp.float32)
    scale = lax.rsqrt(jnp.mean(values * values, axis=-1, keepdims=True) + EPSILON)
    return (values * scale * gain).astype(jnp.bfloat16)


def expert_half(token_rows, weights_gu, weights_dn):
    units = weights_dn.shape[0]
    joined = jnp.dot(token_rows, weights_gu, preferred_element_type=jnp.float32)
    hidden = (jax.nn.silu(joined[:, :units]) * joined[:, units:]).astype(jnp.bfloat16)
    partial_out = jnp.dot(hidden, weights_dn, preferred_element_type=jnp.float32)
    return partial_out.astype(jnp.bfloat16)


def local(tokens, routes, combine_weights, norm_gain, gate_up, down):
    inputs = tokens[0]
    micro, tok_count, width = inputs.shape
    experts = lax.axis_size("expert") // 2
    mine = lax.axis_index("expert") // 2
    normed = normalize(inputs, norm_gain[0])
    names = jnp.arange(experts, dtype=routes.dtype)
    chosen = routes[0][..., None] == names
    table = jnp.sum(jnp.where(chosen, combine_weights[0][..., None], 0.0), axis=2)
    every = lax.all_gather(normed, "expert", axis=1, tiled=True)
    tables = lax.all_gather(table, "expert", axis=1, tiled=True)
    weights = jnp.sum(jnp.where(names == mine, tables, 0.0), axis=-1)
    rows = every.reshape(-1, width)
    partial_out = expert_half(rows, gate_up[0, 0], down[0, 0])
    scaled = weights.reshape(-1, 1) * partial_out.astype(jnp.float32)
    scaled = scaled.astype(jnp.bfloat16).reshape(micro, -1, width)
    summed = lax.psum_scatter(scaled, "expert", scatter_dimension=1, tiled=True)
    mixed = inputs.astype(jnp.float32) + summed.astype(jnp.float32)
    moved = from_behind(mixed.astype(jnp.bfloat16), "section", 1)
    return moved[None]


def solution(mesh):
    return jax.shard_map(
        local,
        mesh=mesh,
        in_specs=(
            P("section", None, "expert", None),
            P("section", None, "expert", None),
            P("section", None, "expert", None),
            P("section", None),
            P("section", "expert", None, None),
            P("section", "expert", None, None),
        ),
        out_specs=P("section", None, "expert", None),
        check_vma=False,
    )
```

```python
import jax
import jax.numpy as jnp
from jax import lax
from jax.sharding import PartitionSpec as P

EPSILON = 1e-06


def from_behind(value, axis, steps):
    count = lax.axis_size(axis)
    pairs = [(source, (source + steps) % count) for source in range(count)]
    return lax.ppermute(value, axis, pairs)


def normalize(block, gain):
    values = block.astype(jnp.float32)
    scale = lax.rsqrt(jnp.mean(values * values, axis=-1, keepdims=True) + EPSILON)
    return (values * scale * gain).astype(jnp.bfloat16)


def expert_half(token_rows, weights_gu, weights_dn):
    units = weights_dn.shape[0]
    joined = jnp.dot(token_rows, weights_gu, preferred_element_type=jnp.float32)
    hidden = (jax.nn.silu(joined[:, :units]) * joined[:, units:]).astype(jnp.bfloat16)
    partial_out = jnp.dot(hidden, weights_dn, preferred_element_type=jnp.float32)
    return partial_out.astype(jnp.bfloat16)


def local(tokens, routes, combine_weights, norm_gain, gate_up, down):
    inputs = tokens[0]
    micro, tok_count, width = inputs.shape
    experts = lax.axis_size("expert") // 2
    mine = lax.axis_index("expert") // 2
    normed = normalize(inputs, norm_gain[0])
    names = jnp.arange(experts, dtype=routes.dtype)
    chosen = routes[0][..., None] == names
    table = jnp.sum(jnp.where(chosen, combine_weights[0][..., None], 0.0), axis=2)
    high = table.astype(jnp.bfloat16)
    low = (table - high.astype(jnp.float32)).astype(jnp.bfloat16)
    spare = jnp.zeros((micro, tok_count, 128 - 2 * experts), jnp.bfloat16)
    packed = jnp.concatenate([normed, high, low, spare], axis=-1)
    every = lax.all_gather(packed, "expert", axis=1, tiled=True)
    tables = every[..., width : width + experts].astype(jnp.float32)
    tables = tables + every[..., width + experts : width + 2 * experts].astype(jnp.float32)
    weights = jnp.sum(jnp.where(names == mine, tables, 0.0), axis=-1)
    rows = every[..., :width].reshape(-1, width)
    partial_out = expert_half(rows, gate_up[0, 0], down[0, 0])
    scaled = weights.reshape(-1, 1) * partial_out.astype(jnp.float32)
    scaled = scaled.astype(jnp.bfloat16).reshape(micro, -1, width)
    summed = lax.psum_scatter(scaled, "expert", scatter_dimension=1, tiled=True)
    mixed = inputs.astype(jnp.float32) + summed.astype(jnp.float32)
    moved = from_behind(mixed.astype(jnp.bfloat16), "section", 1)
    return moved[None]


def solution(mesh):
    return jax.shard_map(
        local,
        mesh=mesh,
        in_specs=(
            P("section", None, "expert", None),
            P("section", None, "expert", None),
            P("section", None, "expert", None),
            P("section", None),
            P("section", "expert", None, None),
            P("section", "expert", None, None),
        ),
        out_specs=P("section", None, "expert", None),
        check_vma=False,
    )
```

```python
import jax
import jax.numpy as jnp
from jax import lax
from jax.sharding import Mesh
from jax.sharding import PartitionSpec as P

EPSILON = 1e-06


def from_behind(value, axis, steps):
    count = lax.axis_size(axis)
    pairs = [(source, (source + steps) % count) for source in range(count)]
    return lax.ppermute(value, axis, pairs)


def swap_cores(value):
    return lax.ppermute(value, "core", [(0, 1), (1, 0)])


def slot_codes(route_block, experts, capacity):
    flat = route_block.reshape(-1)
    onehot = (flat[:, None] == jnp.arange(experts, dtype=jnp.int32)[None, :]).astype(jnp.int32)
    before = jnp.cumsum(onehot, axis=0) - onehot
    slot = jnp.sum(before * onehot, axis=1)
    return (flat * capacity + slot).reshape(route_block.shape)


def normalize(block, gain):
    values = block.astype(jnp.float32)
    scale = lax.rsqrt(jnp.mean(values * values, axis=-1, keepdims=True) + EPSILON)
    return (values * scale * gain).astype(jnp.bfloat16)


def expert_half(token_rows, weights_gu, weights_dn):
    units = weights_dn.shape[0]
    joined = jnp.dot(token_rows, weights_gu, preferred_element_type=jnp.float32)
    hidden = (jax.nn.silu(joined[:, :units]) * joined[:, units:]).astype(jnp.bfloat16)
    partial_out = jnp.dot(hidden, weights_dn, preferred_element_type=jnp.float32)
    return partial_out.astype(jnp.bfloat16)


def local(tokens, routes, combine_weights, norm_gain, gate_up, down):
    inputs = tokens[0]
    micro, tok_count, width = inputs.shape
    experts = lax.axis_size("z")
    topk = routes.shape[3]
    capacity = 2 * ((3 * tok_count * topk + 4 * experts - 1) // (4 * experts))
    normed = normalize(inputs, norm_gain[0])
    codes = jax.vmap(lambda block: slot_codes(block, experts, capacity))(routes[0])
    lanes = jnp.arange(experts * capacity, dtype=jnp.int32)
    onehot = jnp.any(codes[..., None] == lanes, axis=2).astype(jnp.bfloat16)
    buffer = jnp.einsum("mtq,mtd->qmd", onehot, normed, preferred_element_type=jnp.float32)
    buffer = buffer.astype(jnp.bfloat16).reshape(experts, capacity, micro, width)
    incoming = lax.all_to_all(buffer, "z", split_axis=0, concat_axis=0, tiled=True)
    rows = jnp.stack([incoming, swap_cores(incoming)]).reshape(-1, width)
    parts = expert_half(rows, gate_up[0, 0], down[0, 0])
    parts = parts.reshape((2,) + incoming.shape)
    other_half = swap_cores(parts[1])
    results = (parts[0].astype(jnp.float32) + other_half.astype(jnp.float32)).astype(jnp.bfloat16)
    returned = lax.all_to_all(results, "z", split_axis=0, concat_axis=0, tiled=True)
    table = jnp.swapaxes(returned.reshape(experts * capacity, micro, width), 0, 1)
    flat_codes = codes.reshape(micro, tok_count * topk)
    picked = table[jnp.arange(micro)[:, None], flat_codes].reshape(micro, tok_count, topk, width)
    mixed = inputs.astype(jnp.float32) + jnp.sum(
        combine_weights[0][..., None] * picked.astype(jnp.float32), axis=2
    )
    moved = from_behind(mixed.astype(jnp.bfloat16), "section", 1)
    return moved[None]


def solution(mesh):
    sections, spread = mesh.devices.shape
    chips = Mesh(mesh.devices.reshape(sections, spread // 2, 2), ("section", "z", "core"))
    split = ("z", "core")
    return jax.shard_map(
        local,
        mesh=chips,
        in_specs=(
            P("section", None, split, None),
            P("section", None, split, None),
            P("section", None, split, None),
            P("section", None),
            P("section", split, None, None),
            P("section", split, None, None),
        ),
        out_specs=P("section", None, split, None),
        check_vma=False,
    )
```

```python
import jax
import jax.numpy as jnp
from jax import lax
from jax.sharding import Mesh
from jax.sharding import PartitionSpec as P

EPSILON = 1e-06


def from_behind(value, axis, steps):
    count = lax.axis_size(axis)
    pairs = [(source, (source + steps) % count) for source in range(count)]
    return lax.ppermute(value, axis, pairs)


def swap_cores(value):
    return lax.ppermute(value, "core", [(0, 1), (1, 0)])


def slot_codes(route_block, experts, capacity):
    flat = route_block.reshape(-1)
    onehot = (flat[:, None] == jnp.arange(experts, dtype=jnp.int32)[None, :]).astype(jnp.int32)
    before = jnp.cumsum(onehot, axis=0) - onehot
    slot = jnp.sum(before * onehot, axis=1)
    return (flat * capacity + slot).reshape(route_block.shape)


def normalize(block, gain):
    values = block.astype(jnp.float32)
    scale = lax.rsqrt(jnp.mean(values * values, axis=-1, keepdims=True) + EPSILON)
    return (values * scale * gain).astype(jnp.bfloat16)


def expert_half(token_rows, weights_gu, weights_dn):
    units = weights_dn.shape[0]
    joined = jnp.dot(token_rows, weights_gu, preferred_element_type=jnp.float32)
    hidden = (jax.nn.silu(joined[:, :units]) * joined[:, units:]).astype(jnp.bfloat16)
    partial_out = jnp.dot(hidden, weights_dn, preferred_element_type=jnp.float32)
    return partial_out.astype(jnp.bfloat16)


def local(tokens, routes, combine_weights, norm_gain, gate_up, down):
    inputs = tokens[0]
    micro, tok_count, width = inputs.shape
    experts = lax.axis_size("z")
    topk = routes.shape[3]
    capacity = 2 * ((3 * tok_count * topk + 4 * experts - 1) // (4 * experts))
    block = micro * capacity
    normed = normalize(inputs, norm_gain[0]).reshape(-1, width)
    codes = jax.vmap(lambda one: slot_codes(one, experts, capacity))(routes[0])
    chosen = codes // capacity
    place = chosen * block + jnp.arange(micro, dtype=jnp.int32)[:, None, None] * capacity
    place = (place + codes % capacity).reshape(micro * tok_count, topk)
    lanes = jnp.arange(experts * block, dtype=jnp.int32)
    hits = place[..., None] == lanes
    onehot = jnp.any(hits, axis=1).astype(jnp.bfloat16)
    buffer = jnp.einsum("tq,td->qd", onehot, normed, preferred_element_type=jnp.float32)
    buffer = buffer.astype(jnp.bfloat16).reshape(experts, block, width)
    incoming = lax.all_to_all(buffer, "z", split_axis=0, concat_axis=0, tiled=True)
    rows = jnp.concatenate([incoming, swap_cores(incoming)]).reshape(-1, width)
    parts = expert_half(rows, gate_up[0, 0], down[0, 0]).reshape((2,) + incoming.shape)
    other_half = swap_cores(parts[1])
    results = (parts[0].astype(jnp.float32) + other_half.astype(jnp.float32)).astype(jnp.bfloat16)
    returned = lax.all_to_all(results, "z", split_axis=0, concat_axis=0, tiled=True)
    table = returned.reshape(-1, width)
    weights = combine_weights[0].reshape(micro * tok_count, topk)
    mixing = jnp.sum(jnp.where(hits, weights[..., None], 0.0), axis=1)
    high = mixing.astype(jnp.bfloat16)
    low = (mixing - high.astype(jnp.float32)).astype(jnp.bfloat16)
    combined = jnp.dot(high, table, preferred_element_type=jnp.float32)
    combined = combined + jnp.dot(low, table, preferred_element_type=jnp.float32)
    mixed = inputs.astype(jnp.float32) + combined.reshape(micro, tok_count, width)
    moved = from_behind(mixed.astype(jnp.bfloat16), "section", 1)
    return moved[None]


def solution(mesh):
    sections, spread = mesh.devices.shape
    chips = Mesh(mesh.devices.reshape(sections, spread // 2, 2), ("section", "z", "core"))
    split = ("z", "core")
    return jax.shard_map(
        local,
        mesh=chips,
        in_specs=(
            P("section", None, split, None),
            P("section", None, split, None),
            P("section", None, split, None),
            P("section", None),
            P("section", split, None, None),
            P("section", split, None, None),
        ),
        out_specs=P("section", None, split, None),
        check_vma=False,
    )
```

```python
import jax
import jax.numpy as jnp
from jax import lax
from jax.sharding import Mesh
from jax.sharding import PartitionSpec as P

EPSILON = 1e-06


def from_behind(value, axis, steps):
    count = lax.axis_size(axis)
    pairs = [(source, (source + steps) % count) for source in range(count)]
    return lax.ppermute(value, axis, pairs)


def swap_cores(value):
    return lax.ppermute(value, "core", [(0, 1), (1, 0)])


def slot_codes(route_block, experts, capacity):
    flat = route_block.reshape(-1)
    onehot = (flat[:, None] == jnp.arange(experts, dtype=jnp.int32)[None, :]).astype(jnp.int32)
    before = jnp.cumsum(onehot, axis=0) - onehot
    slot = jnp.sum(before * onehot, axis=1)
    return (flat * capacity + slot).reshape(route_block.shape)


def normalize(block, gain):
    values = block.astype(jnp.float32)
    scale = lax.rsqrt(jnp.mean(values * values, axis=-1, keepdims=True) + EPSILON)
    return (values * scale * gain).astype(jnp.bfloat16)


def expert_half(token_rows, weights_gu, weights_dn):
    units = weights_dn.shape[0]
    joined = jnp.dot(token_rows, weights_gu, preferred_element_type=jnp.float32)
    hidden = (jax.nn.silu(joined[:, :units]) * joined[:, units:]).astype(jnp.bfloat16)
    partial_out = jnp.dot(hidden, weights_dn, preferred_element_type=jnp.float32)
    return partial_out.astype(jnp.bfloat16)


def local(tokens, routes, combine_weights, norm_gain, gate_up, down):
    inputs = tokens[0]
    micro, tok_count, width = inputs.shape
    experts = lax.axis_size("z")
    topk = routes.shape[3]
    capacity = 2 * ((3 * tok_count * topk + 4 * experts - 1) // (4 * experts))
    block = micro * capacity
    normed = normalize(inputs, norm_gain[0]).reshape(-1, width)
    codes = jax.vmap(lambda one: slot_codes(one, experts, capacity))(routes[0])
    chosen = codes // capacity
    place = chosen * block + jnp.arange(micro, dtype=jnp.int32)[:, None, None] * capacity
    place = (place + codes % capacity).reshape(micro * tok_count, topk)
    lanes = jnp.arange(experts * block, dtype=jnp.int32)
    hits = place[..., None] == lanes
    onehot = jnp.any(hits, axis=1).astype(jnp.bfloat16)
    buffer = jnp.einsum("tq,td->qd", onehot, normed, preferred_element_type=jnp.float32)
    buffer = buffer.astype(jnp.bfloat16).reshape(experts, block, width)
    incoming = lax.all_to_all(buffer, "z", split_axis=0, concat_axis=0, tiled=True)
    partner_rows = swap_cores(incoming)
    own = expert_half(incoming.reshape(-1, width), gate_up[0, 0], down[0, 0])
    lent = expert_half(partner_rows.reshape(-1, width), gate_up[0, 0], down[0, 0])
    other_half = swap_cores(lent.reshape(incoming.shape))
    results = (own.reshape(incoming.shape).astype(jnp.float32) + other_half.astype(jnp.float32))
    results = results.astype(jnp.bfloat16)
    returned = lax.all_to_all(results, "z", split_axis=0, concat_axis=0, tiled=True)
    table = returned.reshape(-1, width)
    weights = combine_weights[0].reshape(micro * tok_count, topk)
    mixing = jnp.sum(jnp.where(hits, weights[..., None], 0.0), axis=1)
    combined = jnp.dot(
        mixing,
        table.astype(jnp.float32),
        precision=lax.Precision.HIGHEST,
        preferred_element_type=jnp.float32,
    )
    mixed = inputs.astype(jnp.float32) + combined.reshape(micro, tok_count, width)
    moved = from_behind(mixed.astype(jnp.bfloat16), "section", 1)
    return moved[None]


def solution(mesh):
    sections, spread = mesh.devices.shape
    chips = Mesh(mesh.devices.reshape(sections, spread // 2, 2), ("section", "z", "core"))
    split = ("z", "core")
    return jax.shard_map(
        local,
        mesh=chips,
        in_specs=(
            P("section", None, split, None),
            P("section", None, split, None),
            P("section", None, split, None),
            P("section", None),
            P("section", split, None, None),
            P("section", split, None, None),
        ),
        out_specs=P("section", None, split, None),
        check_vma=False,
    )
```

```python
import jax
import jax.numpy as jnp
from jax import lax
from jax.sharding import Mesh
from jax.sharding import PartitionSpec as P

EPSILON = 1e-06


def from_behind(value, axis, steps):
    count = lax.axis_size(axis)
    pairs = [(source, (source + steps) % count) for source in range(count)]
    return lax.ppermute(value, axis, pairs)


def swap_cores(value):
    return lax.ppermute(value, "core", [(0, 1), (1, 0)])


def slot_codes(route_block, experts, capacity):
    flat = route_block.reshape(-1)
    onehot = (flat[:, None] == jnp.arange(experts, dtype=jnp.int32)[None, :]).astype(jnp.int32)
    before = jnp.cumsum(onehot, axis=0) - onehot
    slot = jnp.sum(before * onehot, axis=1)
    return (flat * capacity + slot).reshape(route_block.shape)


def normalize(block, gain):
    values = block.astype(jnp.float32)
    scale = lax.rsqrt(jnp.mean(values * values, axis=-1, keepdims=True) + EPSILON)
    return (values * scale * gain).astype(jnp.bfloat16)


def expert_half(token_rows, weights_gu, weights_dn):
    units = weights_dn.shape[0]
    joined = jnp.dot(token_rows, weights_gu, preferred_element_type=jnp.float32)
    hidden = (jax.nn.silu(joined[:, :units]) * joined[:, units:]).astype(jnp.bfloat16)
    partial_out = jnp.dot(hidden, weights_dn, preferred_element_type=jnp.float32)
    return partial_out.astype(jnp.bfloat16)


def local(tokens, routes, combine_weights, norm_gain, gate_up, down):
    inputs = tokens[0]
    micro, tok_count, width = inputs.shape
    experts = lax.axis_size("z")
    topk = routes.shape[3]
    capacity = 2 * ((3 * tok_count * topk + 4 * experts - 1) // (4 * experts))
    block = micro * capacity
    normed = normalize(inputs, norm_gain[0]).reshape(-1, width)
    codes = jax.vmap(lambda one: slot_codes(one, experts, capacity))(routes[0])
    chosen = codes // capacity
    place = chosen * block + jnp.arange(micro, dtype=jnp.int32)[:, None, None] * capacity
    place = (place + codes % capacity).reshape(micro * tok_count, topk)
    lanes = jnp.arange(experts * block, dtype=jnp.int32)
    hits = place[..., None] == lanes
    onehot = jnp.any(hits, axis=1).astype(jnp.bfloat16)
    buffer = jnp.einsum("tq,td->qd", onehot, normed, preferred_element_type=jnp.float32)
    buffer = buffer.astype(jnp.bfloat16).reshape(experts, block, width)
    incoming = lax.all_to_all(buffer, "z", split_axis=0, concat_axis=0, tiled=True)
    partner_rows = swap_cores(incoming)
    own = expert_half(incoming.reshape(-1, width), gate_up[0, 0], down[0, 0])
    lent = expert_half(partner_rows.reshape(-1, width), gate_up[0, 0], down[0, 0])
    other_half = swap_cores(lent.reshape(incoming.shape))
    results = (own.reshape(incoming.shape).astype(jnp.float32) + other_half.astype(jnp.float32))
    results = results.astype(jnp.bfloat16)
    weights = combine_weights[0].reshape(micro * tok_count, topk)
    mixing = jnp.sum(jnp.where(hits, weights[..., None], 0.0), axis=1)
    ahead_inputs = from_behind(inputs, "section", 1)
    ahead_mixing = from_behind(mixing, "section", 1)
    sections = lax.axis_size("section")
    chip = lax.axis_index("z")
    combined = jnp.zeros((micro * tok_count, width), jnp.float32)
    for shift in range(1 - experts, experts):
        target = jnp.clip(chip + shift, 0, experts - 1)
        piece = lax.dynamic_index_in_dim(results, target, 0, keepdims=False)
        pairs = [
            (here * experts + lane, ((here + 1) % sections) * experts + lane + shift)
            for here in range(sections)
            for lane in range(experts)
            if 0 <= lane + shift < experts
        ]
        got = lax.ppermute(piece, ("section", "z"), pairs)
        source = jnp.clip(chip - shift, 0, experts - 1)
        columns = lax.dynamic_slice_in_dim(ahead_mixing, source * block, block, axis=1)
        combined = combined + jnp.dot(
            columns,
            got.astype(jnp.float32),
            precision=lax.Precision.HIGHEST,
            preferred_element_type=jnp.float32,
        )
    mixed = ahead_inputs.astype(jnp.float32) + combined.reshape(micro, tok_count, width)
    return mixed.astype(jnp.bfloat16)[None]


def solution(mesh):
    sections, spread = mesh.devices.shape
    chips = Mesh(mesh.devices.reshape(sections, spread // 2, 2), ("section", "z", "core"))
    split = ("z", "core")
    return jax.shard_map(
        local,
        mesh=chips,
        in_specs=(
            P("section", None, split, None),
            P("section", None, split, None),
            P("section", None, split, None),
            P("section", None),
            P("section", split, None, None),
            P("section", split, None, None),
        ),
        out_specs=P("section", None, split, None),
        check_vma=False,
    )
```

```python
import jax
import jax.numpy as jnp
from jax import lax
from jax.sharding import Mesh
from jax.sharding import PartitionSpec as P

EPSILON = 1e-06


def from_behind(value, axis, steps):
    count = lax.axis_size(axis)
    pairs = [(source, (source + steps) % count) for source in range(count)]
    return lax.ppermute(value, axis, pairs)


def swap_cores(value):
    return lax.ppermute(value, "core", [(0, 1), (1, 0)])


def slot_codes(route_block, experts, capacity):
    flat = route_block.reshape(-1)
    onehot = (flat[:, None] == jnp.arange(experts, dtype=jnp.int32)[None, :]).astype(jnp.int32)
    before = jnp.cumsum(onehot, axis=0) - onehot
    slot = jnp.sum(before * onehot, axis=1)
    return (flat * capacity + slot).reshape(route_block.shape)


def normalize(block, gain):
    values = block.astype(jnp.float32)
    scale = lax.rsqrt(jnp.mean(values * values, axis=-1, keepdims=True) + EPSILON)
    return (values * scale * gain).astype(jnp.bfloat16)


def expert_half(token_rows, weights_gu, weights_dn):
    units = weights_dn.shape[0]
    joined = jnp.dot(token_rows, weights_gu, preferred_element_type=jnp.float32)
    hidden = (jax.nn.silu(joined[:, :units]) * joined[:, units:]).astype(jnp.bfloat16)
    partial_out = jnp.dot(hidden, weights_dn, preferred_element_type=jnp.float32)
    return partial_out.astype(jnp.bfloat16)


def one_micro(inputs, normed, codes, weights, gate_up, down, experts, capacity):
    width = inputs.shape[-1]
    lanes = jnp.arange(experts * capacity, dtype=jnp.int32)
    hits = codes[..., None] == lanes
    onehot = jnp.any(hits, axis=1).astype(jnp.bfloat16)
    buffer = jnp.einsum("tq,td->qd", onehot, normed, preferred_element_type=jnp.float32)
    buffer = buffer.astype(jnp.bfloat16).reshape(experts, capacity, width)
    incoming = lax.all_to_all(buffer, "z", split_axis=0, concat_axis=0, tiled=True)
    partner_rows = swap_cores(incoming)
    own = expert_half(incoming.reshape(-1, width), gate_up, down)
    lent = expert_half(partner_rows.reshape(-1, width), gate_up, down)
    other_half = swap_cores(lent.reshape(incoming.shape))
    results = (own.reshape(incoming.shape).astype(jnp.float32) + other_half.astype(jnp.float32))
    results = results.astype(jnp.bfloat16)
    returned = lax.all_to_all(results, "z", split_axis=0, concat_axis=0, tiled=True)
    table = returned.reshape(-1, width)
    mixing = jnp.sum(jnp.where(hits, weights[..., None], 0.0), axis=1)
    combined = jnp.dot(
        mixing,
        table.astype(jnp.float32),
        precision=lax.Precision.HIGHEST,
        preferred_element_type=jnp.float32,
    )
    mixed = inputs.astype(jnp.float32) + combined
    return from_behind(mixed.astype(jnp.bfloat16), "section", 1)


def local(tokens, routes, combine_weights, norm_gain, gate_up, down):
    inputs = tokens[0]
    micro, tok_count, width = inputs.shape
    experts = lax.axis_size("z")
    topk = routes.shape[3]
    capacity = 2 * ((3 * tok_count * topk + 4 * experts - 1) // (4 * experts))
    normed = normalize(inputs, norm_gain[0])
    codes = jax.vmap(lambda one: slot_codes(one, experts, capacity))(routes[0])
    pieces = [
        one_micro(
            inputs[m],
            normed[m],
            codes[m],
            combine_weights[0, m],
            gate_up[0, 0],
            down[0, 0],
            experts,
            capacity,
        )
        for m in range(micro)
    ]
    return jnp.stack(pieces)[None]


def solution(mesh):
    sections, spread = mesh.devices.shape
    chips = Mesh(mesh.devices.reshape(sections, spread // 2, 2), ("section", "z", "core"))
    split = ("z", "core")
    return jax.shard_map(
        local,
        mesh=chips,
        in_specs=(
            P("section", None, split, None),
            P("section", None, split, None),
            P("section", None, split, None),
            P("section", None),
            P("section", split, None, None),
            P("section", split, None, None),
        ),
        out_specs=P("section", None, split, None),
        check_vma=False,
    )
```

```python
import jax
import jax.numpy as jnp
from jax import lax
from jax.sharding import Mesh
from jax.sharding import PartitionSpec as P

EPSILON = 1e-06


def from_behind(value, axis, steps):
    count = lax.axis_size(axis)
    pairs = [(source, (source + steps) % count) for source in range(count)]
    return lax.ppermute(value, axis, pairs)


def swap_cores(value):
    return lax.ppermute(value, "core", [(0, 1), (1, 0)])


def slot_codes(route_block, experts, capacity):
    flat = route_block.reshape(-1)
    count = flat.shape[0]
    onehot = (flat[:, None] == jnp.arange(experts, dtype=flat.dtype)[None, :]).astype(jnp.bfloat16)
    order = jnp.arange(count, dtype=jnp.int32)
    earlier = (order[:, None] > order[None, :]).astype(jnp.bfloat16)
    before = jnp.dot(earlier, onehot, preferred_element_type=jnp.float32)
    slot = jnp.sum(before * onehot.astype(jnp.float32), axis=1).astype(jnp.int32)
    return (flat * capacity + slot).reshape(route_block.shape)


def normalize(block, gain):
    values = block.astype(jnp.float32)
    scale = lax.rsqrt(jnp.mean(values * values, axis=-1, keepdims=True) + EPSILON)
    return (values * scale * gain).astype(jnp.bfloat16)


def expert_half(token_rows, weights_gu, weights_dn):
    units = weights_dn.shape[0]
    joined = jnp.dot(token_rows, weights_gu, preferred_element_type=jnp.float32)
    hidden = (jax.nn.silu(joined[:, :units]) * joined[:, units:]).astype(jnp.bfloat16)
    partial_out = jnp.dot(hidden, weights_dn, preferred_element_type=jnp.float32)
    return partial_out.astype(jnp.bfloat16)


def local(tokens, routes, combine_weights, norm_gain, gate_up, down):
    inputs = tokens[0]
    micro, tok_count, width = inputs.shape
    experts = lax.axis_size("z")
    topk = routes.shape[3]
    capacity = 2 * ((3 * tok_count * topk + 4 * experts - 1) // (4 * experts))
    block = micro * capacity
    normed = normalize(inputs, norm_gain[0]).reshape(-1, width)
    codes = jax.vmap(lambda one: slot_codes(one, experts, capacity))(routes[0])
    chosen = codes // capacity
    place = chosen * block + jnp.arange(micro, dtype=jnp.int32)[:, None, None] * capacity
    place = (place + codes % capacity).reshape(micro * tok_count, topk)
    lanes = jnp.arange(experts * block, dtype=jnp.int32)
    hits = place[..., None] == lanes
    onehot = jnp.any(hits, axis=1).astype(jnp.bfloat16)
    buffer = jnp.einsum("tq,td->qd", onehot, normed, preferred_element_type=jnp.float32)
    buffer = buffer.astype(jnp.bfloat16).reshape(experts, block, width)
    incoming = lax.all_to_all(buffer, "z", split_axis=0, concat_axis=0, tiled=True)
    partner_rows = swap_cores(incoming)
    own = expert_half(incoming.reshape(-1, width), gate_up[0, 0], down[0, 0])
    lent = expert_half(partner_rows.reshape(-1, width), gate_up[0, 0], down[0, 0])
    other_half = swap_cores(lent.reshape(incoming.shape))
    results = (own.reshape(incoming.shape).astype(jnp.float32) + other_half.astype(jnp.float32))
    results = results.astype(jnp.bfloat16)
    returned = lax.all_to_all(results, "z", split_axis=0, concat_axis=0, tiled=True)
    table = returned.reshape(-1, width)
    weights = combine_weights[0].reshape(micro * tok_count, topk)
    mixing = jnp.sum(jnp.where(hits, weights[..., None], 0.0), axis=1)
    high = lax.reduce_precision(mixing, exponent_bits=8, mantissa_bits=7)
    low = (mixing - high).astype(jnp.bfloat16)
    combined = jnp.dot(high.astype(jnp.bfloat16), table, preferred_element_type=jnp.float32)
    combined = combined + jnp.dot(low, table, preferred_element_type=jnp.float32)
    mixed = inputs.astype(jnp.float32) + combined.reshape(micro, tok_count, width)
    moved = from_behind(mixed.astype(jnp.bfloat16), "section", 1)
    return moved[None]


def solution(mesh):
    sections, spread = mesh.devices.shape
    chips = Mesh(mesh.devices.reshape(sections, spread // 2, 2), ("section", "z", "core"))
    split = ("z", "core")
    return jax.shard_map(
        local,
        mesh=chips,
        in_specs=(
            P("section", None, split, None),
            P("section", None, split, None),
            P("section", None, split, None),
            P("section", None),
            P("section", split, None, None),
            P("section", split, None, None),
        ),
        out_specs=P("section", None, split, None),
        check_vma=False,
    )
```

```python
import jax
import jax.numpy as jnp
from jax import lax
from jax.experimental import pallas as pl
from jax.sharding import Mesh
from jax.sharding import PartitionSpec as P

EPSILON = 1e-06


def from_behind(value, axis, steps):
    count = lax.axis_size(axis)
    pairs = [(source, (source + steps) % count) for source in range(count)]
    return lax.ppermute(value, axis, pairs)


def swap_cores(value):
    return lax.ppermute(value, "core", [(0, 1), (1, 0)])


def expert_half(token_rows, weights_gu, weights_dn):
    units = weights_dn.shape[0]
    joined = jnp.dot(token_rows, weights_gu, preferred_element_type=jnp.float32)
    hidden = (jax.nn.silu(joined[:, :units]) * joined[:, units:]).astype(jnp.bfloat16)
    partial_out = jnp.dot(hidden, weights_dn, preferred_element_type=jnp.float32)
    return partial_out.astype(jnp.bfloat16)


def prepare_kernel(x_ref, gain_ref, route_ref, weight_ref, buffer_ref, mixing_ref, *, micro, experts, capacity):
    rows, _ = x_ref.shape
    topk = route_ref.shape[1]
    tok_count = rows // micro
    block = micro * capacity
    slots = experts * block
    values = x_ref[...].astype(jnp.float32)
    scale = lax.rsqrt(jnp.mean(values * values, axis=-1, keepdims=True) + EPSILON)
    normed = (values * scale * gain_ref[...]).astype(jnp.bfloat16)
    routes = route_ref[...]
    weights = weight_ref[...]
    down_ix = lax.broadcasted_iota(jnp.int32, (rows, rows), 0)
    across = lax.broadcasted_iota(jnp.int32, (rows, rows), 1)
    group_down = jnp.zeros((rows, rows), jnp.int32)
    group_across = jnp.zeros((rows, rows), jnp.int32)
    group_row = jnp.zeros((rows, 1), jnp.int32)
    row_ix = lax.broadcasted_iota(jnp.int32, (rows, 1), 0)
    for m in range(1, micro):
        group_down = group_down + (down_ix >= m * tok_count).astype(jnp.int32)
        group_across = group_across + (across >= m * tok_count).astype(jnp.int32)
        group_row = group_row + (row_ix >= m * tok_count).astype(jnp.int32)
    earlier = ((group_down == group_across) & (across < down_ix)).astype(jnp.bfloat16)
    names = lax.broadcasted_iota(jnp.int32, (rows, experts), 1)
    picks = [(routes[:, k : k + 1] == names).astype(jnp.float32) for k in range(topk)]
    total = picks[0]
    for k in range(1, topk):
        total = total + picks[k]
    before = jnp.dot(earlier, total.astype(jnp.bfloat16), preferred_element_type=jnp.float32)
    lanes = lax.broadcasted_iota(jnp.int32, (rows, slots), 1)
    hit = jnp.zeros((rows, slots), jnp.float32)
    mixing = jnp.zeros((rows, slots), jnp.float32)
    for k in range(topk):
        slot = jnp.sum(before * picks[k], axis=1, keepdims=True).astype(jnp.int32)
        place = routes[:, k : k + 1] * block + group_row * capacity + slot
        match = place == lanes
        hit = jnp.maximum(hit, match.astype(jnp.float32))
        mixing = mixing + jnp.where(match, weights[:, k : k + 1], 0.0)
        before = before + picks[k]
    buffer = lax.dot_general(
        hit.astype(jnp.bfloat16),
        normed,
        (((0,), (0,)), ((), ())),
        preferred_element_type=jnp.float32,
    )
    buffer_ref[...] = buffer.astype(jnp.bfloat16)
    mixing_ref[...] = mixing


def prepare(inputs, gain, routes, weights, experts, capacity):
    micro, tok_count, width = inputs.shape
    rows = micro * tok_count
    slots = experts * micro * capacity
    return pl.pallas_call(
        lambda *refs: prepare_kernel(*refs, micro=micro, experts=experts, capacity=capacity),
        out_shape=(
            jax.ShapeDtypeStruct((slots, width), jnp.bfloat16),
            jax.ShapeDtypeStruct((rows, slots), jnp.float32),
        ),
    )(inputs.reshape(rows, width), gain.reshape(1, width), routes.reshape(rows, -1), weights.reshape(rows, -1))


def body(tokens, routes, combine_weights, norm_gain, gate_up, down):
    inputs = tokens[0]
    micro, tok_count, width = inputs.shape
    experts = lax.axis_size("z")
    topk = routes.shape[3]
    capacity = 2 * ((3 * tok_count * topk + 4 * experts - 1) // (4 * experts))
    block = micro * capacity
    buffer, mixing = prepare(inputs, norm_gain[0], routes[0], combine_weights[0], experts, capacity)
    buffer = buffer.reshape(experts, block, width)
    incoming = lax.all_to_all(buffer, "z", split_axis=0, concat_axis=0, tiled=True)
    partner_rows = swap_cores(incoming)
    own = expert_half(incoming.reshape(-1, width), gate_up[0, 0], down[0, 0])
    lent = expert_half(partner_rows.reshape(-1, width), gate_up[0, 0], down[0, 0])
    other_half = swap_cores(lent.reshape(incoming.shape))
    results = (own.reshape(incoming.shape).astype(jnp.float32) + other_half.astype(jnp.float32))
    results = results.astype(jnp.bfloat16)
    returned = lax.all_to_all(results, "z", split_axis=0, concat_axis=0, tiled=True)
    table = returned.reshape(-1, width)
    combined = jnp.dot(
        mixing,
        table.astype(jnp.float32),
        precision=lax.Precision.HIGHEST,
        preferred_element_type=jnp.float32,
    )
    mixed = inputs.astype(jnp.float32) + combined.reshape(micro, tok_count, width)
    moved = from_behind(mixed.astype(jnp.bfloat16), "section", 1)
    return moved[None]


def solution(mesh):
    sections, spread = mesh.devices.shape
    chips = Mesh(mesh.devices.reshape(sections, spread // 2, 2), ("section", "z", "core"))
    split = ("z", "core")
    return jax.shard_map(
        body,
        mesh=chips,
        in_specs=(
            P("section", None, split, None),
            P("section", None, split, None),
            P("section", None, split, None),
            P("section", None),
            P("section", split, None, None),
            P("section", split, None, None),
        ),
        out_specs=P("section", None, split, None),
        check_vma=False,
    )
```

```python
import jax
import jax.numpy as jnp
from jax import lax
from jax.experimental import pallas as pl
from jax.sharding import Mesh
from jax.sharding import PartitionSpec as P

EPSILON = 1e-06


def from_behind(value, axis, steps):
    count = lax.axis_size(axis)
    pairs = [(source, (source + steps) % count) for source in range(count)]
    return lax.ppermute(value, axis, pairs)


def swap_cores(value):
    return lax.ppermute(value, "core", [(0, 1), (1, 0)])


def expert_up(token_rows, weights_gu, units):
    joined = jnp.dot(token_rows, weights_gu, preferred_element_type=jnp.float32)
    return (jax.nn.silu(joined[:, :units]) * joined[:, units:]).astype(jnp.bfloat16)


def expert_down(hidden, weights_dn):
    partial_out = jnp.dot(hidden, weights_dn, preferred_element_type=jnp.float32)
    return partial_out.astype(jnp.bfloat16)


def prepare_kernel(x_ref, gain_ref, route_ref, weight_ref, buffer_ref, mixing_ref, *, experts, capacity):
    micro, topk, tok_count = route_ref.shape
    width = x_ref.shape[-1]
    block = micro * capacity
    slots = experts * block
    values = x_ref[...].astype(jnp.float32)
    scale = lax.rsqrt(jnp.mean(values * values, axis=-1, keepdims=True) + EPSILON)
    normed = (values * scale * gain_ref[...]).astype(jnp.bfloat16)
    upper = (
        lax.broadcasted_iota(jnp.int32, (tok_count, tok_count), 0)
        < lax.broadcasted_iota(jnp.int32, (tok_count, tok_count), 1)
    ).astype(jnp.float32)
    names = lax.broadcasted_iota(jnp.int32, (experts, tok_count), 0)
    lanes = lax.broadcasted_iota(jnp.int32, (slots, tok_count), 0)
    buffer = jnp.zeros((slots, width), jnp.float32)
    for m in range(micro):
        routes = route_ref[m]
        weights = weight_ref[m]
        offset = jnp.zeros((experts, 1), jnp.float32)
        hit = jnp.zeros((slots, tok_count), jnp.float32)
        mixing = jnp.zeros((slots, tok_count), jnp.float32)
        for k in range(topk):
            chosen = routes[k : k + 1, :]
            pick = (chosen == names).astype(jnp.float32)
            before = jnp.dot(pick, upper, preferred_element_type=jnp.float32) + offset
            slot = jnp.sum(before * pick, axis=0, keepdims=True).astype(jnp.int32)
            place = chosen * block + m * capacity + slot
            match = place == lanes
            hit = jnp.maximum(hit, match.astype(jnp.float32))
            mixing = mixing + jnp.where(match, weights[k : k + 1, :], 0.0)
            offset = offset + jnp.sum(pick, axis=1, keepdims=True)
        rows = normed[m * tok_count : (m + 1) * tok_count, :]
        buffer = buffer + jnp.dot(hit.astype(jnp.bfloat16), rows, preferred_element_type=jnp.float32)
        mixing_ref[m] = mixing
    buffer_ref[...] = buffer.astype(jnp.bfloat16)


def prepare(inputs, gain, routes, weights, experts, capacity):
    micro, tok_count, width = inputs.shape
    slots = experts * micro * capacity
    return pl.pallas_call(
        lambda *refs: prepare_kernel(*refs, experts=experts, capacity=capacity),
        out_shape=(
            jax.ShapeDtypeStruct((slots, width), jnp.bfloat16),
            jax.ShapeDtypeStruct((micro, slots, tok_count), jnp.float32),
        ),
    )(
        inputs.reshape(micro * tok_count, width),
        gain.reshape(1, width),
        jnp.swapaxes(routes, 1, 2),
        jnp.swapaxes(weights, 1, 2),
    )


def body(tokens, routes, combine_weights, norm_gain, gate_up, down):
    inputs = tokens[0]
    micro, tok_count, width = inputs.shape
    experts = lax.axis_size("z")
    topk = routes.shape[3]
    capacity = 2 * ((3 * tok_count * topk + 4 * experts - 1) // (4 * experts))
    block = micro * capacity
    buffer, mixing = prepare(inputs, norm_gain[0], routes[0], combine_weights[0], experts, capacity)
    buffer = buffer.reshape(experts, block, width)
    incoming = lax.all_to_all(buffer, "z", split_axis=0, concat_axis=0, tiled=True)
    units = down.shape[2]
    partner_rows = swap_cores(incoming)
    own_hidden = expert_up(incoming.reshape(-1, width), gate_up[0, 0], units)
    lent_hidden = expert_up(partner_rows.reshape(-1, width), gate_up[0, 0], units)
    lent = expert_down(lent_hidden, down[0, 0])
    other_half = swap_cores(lent.reshape(incoming.shape))
    own = expert_down(own_hidden, down[0, 0])
    results = (own.reshape(incoming.shape).astype(jnp.float32) + other_half.astype(jnp.float32))
    results = results.astype(jnp.bfloat16)
    returned = lax.all_to_all(results, "z", split_axis=0, concat_axis=0, tiled=True)
    table = returned.reshape(-1, width)
    combined = jnp.einsum(
        "mqt,qd->mtd",
        mixing,
        table.astype(jnp.float32),
        precision=lax.Precision.HIGHEST,
        preferred_element_type=jnp.float32,
    )
    mixed = inputs.astype(jnp.float32) + combined
    moved = from_behind(mixed.astype(jnp.bfloat16), "section", 1)
    return moved[None]


def solution(mesh):
    sections, spread = mesh.devices.shape
    chips = Mesh(mesh.devices.reshape(sections, spread // 2, 2), ("section", "z", "core"))
    split = ("z", "core")
    return jax.shard_map(
        body,
        mesh=chips,
        in_specs=(
            P("section", None, split, None),
            P("section", None, split, None),
            P("section", None, split, None),
            P("section", None),
            P("section", split, None, None),
            P("section", split, None, None),
        ),
        out_specs=P("section", None, split, None),
        check_vma=False,
    )
```

```python
import jax
import jax.numpy as jnp
from jax import lax
from jax.experimental import pallas as pl
from jax.sharding import Mesh
from jax.sharding import PartitionSpec as P

EPSILON = 1e-06


def from_behind(value, axis, steps):
    count = lax.axis_size(axis)
    pairs = [(source, (source + steps) % count) for source in range(count)]
    return lax.ppermute(value, axis, pairs)


def swap_cores(value):
    return lax.ppermute(value, "core", [(0, 1), (1, 0)])


def expert_half(token_rows, weights_gu, weights_dn):
    units = weights_dn.shape[0]
    joined = jnp.dot(token_rows, weights_gu, preferred_element_type=jnp.float32)
    hidden = (jax.nn.silu(joined[:, :units]) * joined[:, units:]).astype(jnp.bfloat16)
    partial_out = jnp.dot(hidden, weights_dn, preferred_element_type=jnp.float32)
    return partial_out.astype(jnp.bfloat16)


def prepare_kernel(x_ref, gain_ref, route_ref, weight_ref, buffer_ref, mixing_ref, *, experts, capacity):
    micro, topk, tok_count = route_ref.shape
    width = x_ref.shape[-1]
    block = micro * capacity
    slots = experts * block
    values = x_ref[...].astype(jnp.float32)
    scale = lax.rsqrt(jnp.mean(values * values, axis=-1, keepdims=True) + EPSILON)
    normed = (values * scale * gain_ref[...]).astype(jnp.bfloat16)
    upper = (
        lax.broadcasted_iota(jnp.int32, (tok_count, tok_count), 0)
        < lax.broadcasted_iota(jnp.int32, (tok_count, tok_count), 1)
    ).astype(jnp.float32)
    names = lax.broadcasted_iota(jnp.int32, (experts, tok_count), 0)
    lanes = lax.broadcasted_iota(jnp.int32, (slots, tok_count), 0)
    buffer = jnp.zeros((slots, width), jnp.float32)
    for m in range(micro):
        routes = route_ref[m]
        weights = weight_ref[m]
        offset = jnp.zeros((experts, 1), jnp.float32)
        hit = jnp.zeros((slots, tok_count), jnp.float32)
        mixing = jnp.zeros((slots, tok_count), jnp.float32)
        for k in range(topk):
            chosen = routes[k : k + 1, :]
            pick = (chosen == names).astype(jnp.float32)
            before = jnp.dot(pick, upper, preferred_element_type=jnp.float32) + offset
            slot = jnp.sum(before * pick, axis=0, keepdims=True).astype(jnp.int32)
            place = chosen * block + m * capacity + slot
            match = place == lanes
            hit = jnp.maximum(hit, match.astype(jnp.float32))
            mixing = mixing + jnp.where(match, weights[k : k + 1, :], 0.0)
            offset = offset + jnp.sum(pick, axis=1, keepdims=True)
        rows = normed[m * tok_count : (m + 1) * tok_count, :]
        buffer = buffer + jnp.dot(hit.astype(jnp.bfloat16), rows, preferred_element_type=jnp.float32)
        mixing_ref[m] = mixing
    buffer_ref[...] = buffer.astype(jnp.bfloat16)


def prepare(inputs, gain, routes, weights, experts, capacity):
    micro, tok_count, width = inputs.shape
    slots = experts * micro * capacity
    return pl.pallas_call(
        lambda *refs: prepare_kernel(*refs, experts=experts, capacity=capacity),
        out_shape=(
            jax.ShapeDtypeStruct((slots, width), jnp.bfloat16),
            jax.ShapeDtypeStruct((micro, slots, tok_count), jnp.float32),
        ),
    )(
        inputs.reshape(micro * tok_count, width),
        gain.reshape(1, width),
        jnp.swapaxes(routes, 1, 2),
        jnp.swapaxes(weights, 1, 2),
    )


def body(tokens, routes, combine_weights, norm_gain, gate_up, down):
    inputs = tokens[0]
    micro, tok_count, width = inputs.shape
    experts = lax.axis_size("z")
    topk = routes.shape[3]
    capacity = 2 * ((3 * tok_count * topk + 4 * experts - 1) // (4 * experts))
    block = micro * capacity
    buffer, mixing = prepare(inputs, norm_gain[0], routes[0], combine_weights[0], experts, capacity)
    buffer = buffer.reshape(experts, block, width)
    incoming = lax.all_to_all(buffer, "z", split_axis=0, concat_axis=0, tiled=True)
    partner_rows = swap_cores(incoming)
    own = expert_half(incoming.reshape(-1, width), gate_up[0, 0], down[0, 0])
    lent = expert_half(partner_rows.reshape(-1, width), gate_up[0, 0], down[0, 0])
    other_half = swap_cores(lent.reshape(incoming.shape))
    results = (own.reshape(incoming.shape).astype(jnp.float32) + other_half.astype(jnp.float32))
    results = results.astype(jnp.bfloat16)
    half = width // 2
    moved = []
    for lo, hi in ((0, half), (half, width)):
        returned = lax.all_to_all(results[..., lo:hi], "z", split_axis=0, concat_axis=0, tiled=True)
        table = returned.reshape(-1, hi - lo)
        combined = jnp.einsum(
            "mqt,qd->mtd",
            mixing,
            table.astype(jnp.float32),
            precision=lax.Precision.HIGHEST,
            preferred_element_type=jnp.float32,
        )
        mixed = inputs[..., lo:hi].astype(jnp.float32) + combined
        moved.append(from_behind(mixed.astype(jnp.bfloat16), "section", 1))
    return jnp.concatenate(moved, axis=-1)[None]


def solution(mesh):
    sections, spread = mesh.devices.shape
    chips = Mesh(mesh.devices.reshape(sections, spread // 2, 2), ("section", "z", "core"))
    split = ("z", "core")
    return jax.shard_map(
        body,
        mesh=chips,
        in_specs=(
            P("section", None, split, None),
            P("section", None, split, None),
            P("section", None, split, None),
            P("section", None),
            P("section", split, None, None),
            P("section", split, None, None),
        ),
        out_specs=P("section", None, split, None),
        check_vma=False,
    )
```

```python
import jax
import jax.numpy as jnp
from jax import lax
from jax.experimental import pallas as pl
from jax.sharding import Mesh
from jax.sharding import PartitionSpec as P

EPSILON = 1e-06


def from_behind(value, axis, steps):
    count = lax.axis_size(axis)
    pairs = [(source, (source + steps) % count) for source in range(count)]
    return lax.ppermute(value, axis, pairs)


def swap_cores(value):
    return lax.ppermute(value, "core", [(0, 1), (1, 0)])


def expert_half(token_rows, weights_gu, weights_dn):
    units = weights_dn.shape[0]
    joined = jnp.dot(token_rows, weights_gu, preferred_element_type=jnp.float32)
    hidden = (jax.nn.silu(joined[:, :units]) * joined[:, units:]).astype(jnp.bfloat16)
    partial_out = jnp.dot(hidden, weights_dn, preferred_element_type=jnp.float32)
    return partial_out.astype(jnp.bfloat16)


def prepare_kernel(x_ref, gain_ref, route_ref, weight_ref, buffer_ref, mixing_ref, *, experts, capacity):
    micro, topk, tok_count = route_ref.shape
    width = x_ref.shape[-1]
    block = micro * capacity
    slots = experts * block
    values = x_ref[...].astype(jnp.float32)
    scale = lax.rsqrt(jnp.mean(values * values, axis=-1, keepdims=True) + EPSILON)
    normed = (values * scale * gain_ref[...]).astype(jnp.bfloat16)
    upper = (
        lax.broadcasted_iota(jnp.int32, (tok_count, tok_count), 0)
        < lax.broadcasted_iota(jnp.int32, (tok_count, tok_count), 1)
    ).astype(jnp.float32)
    names = lax.broadcasted_iota(jnp.int32, (experts, tok_count), 0)
    lanes = lax.broadcasted_iota(jnp.int32, (slots, tok_count), 0)
    buffer = jnp.zeros((slots, width), jnp.float32)
    for m in range(micro):
        routes = route_ref[m]
        weights = weight_ref[m]
        offset = jnp.zeros((experts, 1), jnp.float32)
        hit = jnp.zeros((slots, tok_count), jnp.float32)
        mixing = jnp.zeros((slots, tok_count), jnp.float32)
        for k in range(topk):
            chosen = routes[k : k + 1, :]
            pick = (chosen == names).astype(jnp.float32)
            before = jnp.dot(pick, upper, preferred_element_type=jnp.float32) + offset
            slot = jnp.sum(before * pick, axis=0, keepdims=True).astype(jnp.int32)
            place = chosen * block + m * capacity + slot
            match = place == lanes
            hit = jnp.maximum(hit, match.astype(jnp.float32))
            mixing = mixing + jnp.where(match, weights[k : k + 1, :], 0.0)
            offset = offset + jnp.sum(pick, axis=1, keepdims=True)
        rows = normed[m * tok_count : (m + 1) * tok_count, :]
        buffer = buffer + jnp.dot(hit.astype(jnp.bfloat16), rows, preferred_element_type=jnp.float32)
        mixing_ref[m] = mixing
    buffer_ref[...] = buffer.astype(jnp.bfloat16)


def prepare(inputs, gain, routes, weights, experts, capacity):
    micro, tok_count, width = inputs.shape
    slots = experts * micro * capacity
    return pl.pallas_call(
        lambda *refs: prepare_kernel(*refs, experts=experts, capacity=capacity),
        out_shape=(
            jax.ShapeDtypeStruct((slots, width), jnp.bfloat16),
            jax.ShapeDtypeStruct((micro, slots, tok_count), jnp.float32),
        ),
    )(
        inputs.reshape(micro * tok_count, width),
        gain.reshape(1, width),
        jnp.swapaxes(routes, 1, 2),
        jnp.swapaxes(weights, 1, 2),
    )


def body(tokens, routes, combine_weights, norm_gain, gate_up, down):
    inputs = tokens[0]
    micro, tok_count, width = inputs.shape
    experts = lax.axis_size("z")
    topk = routes.shape[3]
    capacity = 2 * ((3 * tok_count * topk + 4 * experts - 1) // (4 * experts))
    block = micro * capacity
    buffer, mixing = prepare(inputs, norm_gain[0], routes[0], combine_weights[0], experts, capacity)
    buffer = buffer.reshape(experts, block, width)
    incoming = lax.all_to_all(buffer, "z", split_axis=0, concat_axis=0, tiled=True)
    partner_rows = swap_cores(incoming)
    own = expert_half(incoming.reshape(-1, width), gate_up[0, 0], down[0, 0])
    cut = experts // 2
    returned_halves = []
    for lo, hi in ((0, cut), (cut, experts)):
        piece = partner_rows[lo:hi].reshape(-1, width)
        lent = expert_half(piece, gate_up[0, 0], down[0, 0])
        returned_halves.append(swap_cores(lent.reshape((hi - lo,) + incoming.shape[1:])))
    other_half = jnp.concatenate(returned_halves)
    results = (own.reshape(incoming.shape).astype(jnp.float32) + other_half.astype(jnp.float32))
    results = results.astype(jnp.bfloat16)
    returned = lax.all_to_all(results, "z", split_axis=0, concat_axis=0, tiled=True)
    table = returned.reshape(-1, width)
    combined = jnp.einsum(
        "mqt,qd->mtd",
        mixing,
        table.astype(jnp.float32),
        precision=lax.Precision.HIGHEST,
        preferred_element_type=jnp.float32,
    )
    mixed = inputs.astype(jnp.float32) + combined
    moved = from_behind(mixed.astype(jnp.bfloat16), "section", 1)
    return moved[None]


def solution(mesh):
    sections, spread = mesh.devices.shape
    chips = Mesh(mesh.devices.reshape(sections, spread // 2, 2), ("section", "z", "core"))
    split = ("z", "core")
    return jax.shard_map(
        body,
        mesh=chips,
        in_specs=(
            P("section", None, split, None),
            P("section", None, split, None),
            P("section", None, split, None),
            P("section", None),
            P("section", split, None, None),
            P("section", split, None, None),
        ),
        out_specs=P("section", None, split, None),
        check_vma=False,
    )
```

```python
import jax
import jax.numpy as jnp
from jax import lax
from jax.experimental import pallas as pl
from jax.sharding import Mesh
from jax.sharding import PartitionSpec as P

EPSILON = 1e-06


def from_behind(value, axis, steps):
    count = lax.axis_size(axis)
    pairs = [(source, (source + steps) % count) for source in range(count)]
    return lax.ppermute(value, axis, pairs)


def swap_cores(value):
    return lax.ppermute(value, "core", [(0, 1), (1, 0)])


def expert_half(token_rows, weights_gu, weights_dn):
    units = weights_dn.shape[0]
    joined = jnp.dot(token_rows, weights_gu, preferred_element_type=jnp.float32)
    hidden = (jax.nn.silu(joined[:, :units]) * joined[:, units:]).astype(jnp.bfloat16)
    partial_out = jnp.dot(hidden, weights_dn, preferred_element_type=jnp.float32)
    return partial_out.astype(jnp.bfloat16)


def prepare_kernel(x_ref, gain_ref, route_ref, weight_ref, buffer_ref, mixing_ref, *, experts, capacity):
    micro, topk, tok_count = route_ref.shape
    width = x_ref.shape[-1]
    block = micro * capacity
    slots = experts * block
    values = x_ref[...].astype(jnp.float32)
    scale = lax.rsqrt(jnp.mean(values * values, axis=-1, keepdims=True) + EPSILON)
    normed = (values * scale * gain_ref[...]).astype(jnp.bfloat16)
    upper = (
        lax.broadcasted_iota(jnp.int32, (tok_count, tok_count), 0)
        < lax.broadcasted_iota(jnp.int32, (tok_count, tok_count), 1)
    ).astype(jnp.float32)
    names = lax.broadcasted_iota(jnp.int32, (experts, tok_count), 0)
    lanes = lax.broadcasted_iota(jnp.int32, (slots, tok_count), 0)
    buffer = jnp.zeros((slots, width), jnp.float32)
    for m in range(micro):
        routes = route_ref[m]
        weights = weight_ref[m]
        offset = jnp.zeros((experts, 1), jnp.float32)
        hit = jnp.zeros((slots, tok_count), jnp.float32)
        mixing = jnp.zeros((slots, tok_count), jnp.float32)
        for k in range(topk):
            chosen = routes[k : k + 1, :]
            pick = (chosen == names).astype(jnp.float32)
            before = jnp.dot(pick, upper, preferred_element_type=jnp.float32) + offset
            slot = jnp.sum(before * pick, axis=0, keepdims=True).astype(jnp.int32)
            place = chosen * block + m * capacity + slot
            match = place == lanes
            hit = jnp.maximum(hit, match.astype(jnp.float32))
            mixing = mixing + jnp.where(match, weights[k : k + 1, :], 0.0)
            offset = offset + jnp.sum(pick, axis=1, keepdims=True)
        rows = normed[m * tok_count : (m + 1) * tok_count, :]
        buffer = buffer + jnp.dot(hit.astype(jnp.bfloat16), rows, preferred_element_type=jnp.float32)
        mixing_ref[m] = mixing
    buffer_ref[...] = buffer.astype(jnp.bfloat16)


def prepare(inputs, gain, routes, weights, experts, capacity):
    micro, tok_count, width = inputs.shape
    slots = experts * micro * capacity
    return pl.pallas_call(
        lambda *refs: prepare_kernel(*refs, experts=experts, capacity=capacity),
        out_shape=(
            jax.ShapeDtypeStruct((slots, width), jnp.bfloat16),
            jax.ShapeDtypeStruct((micro, slots, tok_count), jnp.float32),
        ),
    )(
        inputs.reshape(micro * tok_count, width),
        gain.reshape(1, width),
        jnp.swapaxes(routes, 1, 2),
        jnp.swapaxes(weights, 1, 2),
    )


def body(tokens, routes, combine_weights, norm_gain, gate_up, down):
    inputs = tokens[0]
    micro, tok_count, width = inputs.shape
    experts = lax.axis_size("z")
    topk = routes.shape[3]
    capacity = 2 * ((3 * tok_count * topk + 4 * experts - 1) // (4 * experts))
    block = micro * capacity
    buffer, mixing = prepare(inputs, norm_gain[0], routes[0], combine_weights[0], experts, capacity)
    buffer = buffer.reshape(experts, block, width)
    incoming = lax.all_to_all(buffer, "z", split_axis=0, concat_axis=0, tiled=True)
    partner_rows = swap_cores(incoming)
    own = expert_half(incoming.reshape(-1, width), gate_up[0, 0], down[0, 0])
    lent = expert_half(partner_rows.reshape(-1, width), gate_up[0, 0], down[0, 0])
    other_half = swap_cores(lent.reshape(incoming.shape))
    results = (own.reshape(incoming.shape).astype(jnp.float32) + other_half.astype(jnp.float32))
    results = results.astype(jnp.bfloat16)
    returned = lax.all_to_all(results, "z", split_axis=0, concat_axis=0, tiled=True)
    table = returned.reshape(-1, width)
    combined = jnp.einsum(
        "mqt,qd->mtd",
        mixing,
        table.astype(jnp.float32),
        precision=lax.Precision.HIGH,
        preferred_element_type=jnp.float32,
    )
    mixed = inputs.astype(jnp.float32) + combined
    moved = from_behind(mixed.astype(jnp.bfloat16), "section", 1)
    return moved[None]


def solution(mesh):
    sections, spread = mesh.devices.shape
    chips = Mesh(mesh.devices.reshape(sections, spread // 2, 2), ("section", "z", "core"))
    split = ("z", "core")
    return jax.shard_map(
        body,
        mesh=chips,
        in_specs=(
            P("section", None, split, None),
            P("section", None, split, None),
            P("section", None, split, None),
            P("section", None),
            P("section", split, None, None),
            P("section", split, None, None),
        ),
        out_specs=P("section", None, split, None),
        check_vma=False,
    )
```

```python
import jax
import jax.numpy as jnp
from jax import lax
from jax.experimental import pallas as pl
from jax.sharding import Mesh
from jax.sharding import PartitionSpec as P

EPSILON = 1e-06


def from_behind(value, axis, steps):
    count = lax.axis_size(axis)
    pairs = [(source, (source + steps) % count) for source in range(count)]
    return lax.ppermute(value, axis, pairs)


def swap_cores(value):
    return lax.ppermute(value, "core", [(0, 1), (1, 0)])


def expert_half(token_rows, weights_gu, weights_dn):
    units = weights_dn.shape[0]
    joined = jnp.dot(token_rows, weights_gu, preferred_element_type=jnp.float32)
    hidden = (jax.nn.silu(joined[:, :units]) * joined[:, units:]).astype(jnp.bfloat16)
    partial_out = jnp.dot(hidden, weights_dn, preferred_element_type=jnp.float32)
    return partial_out.astype(jnp.bfloat16)


def prepare_kernel(x_ref, gain_ref, route_ref, weight_ref, buffer_ref, mixing_ref, *, experts, capacity):
    micro, topk, tok_count = route_ref.shape
    width = x_ref.shape[-1]
    block = micro * capacity
    slots = experts * block
    values = x_ref[...].astype(jnp.float32)
    scale = lax.rsqrt(jnp.mean(values * values, axis=-1, keepdims=True) + EPSILON)
    normed = (values * scale * gain_ref[...]).astype(jnp.bfloat16)
    upper = (
        lax.broadcasted_iota(jnp.int32, (tok_count, tok_count), 0)
        < lax.broadcasted_iota(jnp.int32, (tok_count, tok_count), 1)
    ).astype(jnp.float32)
    names = lax.broadcasted_iota(jnp.int32, (experts, tok_count), 0)
    lanes = lax.broadcasted_iota(jnp.int32, (slots, tok_count), 0)
    columns = lax.broadcasted_iota(jnp.int32, (tok_count, slots), 1)
    buffer = jnp.zeros((slots, width), jnp.float32)
    for m in range(micro):
        routes = route_ref[m]
        weights = weight_ref[m]
        offset = jnp.zeros((experts, 1), jnp.float32)
        hit = jnp.zeros((slots, tok_count), jnp.float32)
        mixing = jnp.zeros((tok_count, slots), jnp.float32)
        for k in range(topk):
            chosen = routes[k : k + 1, :]
            pick = (chosen == names).astype(jnp.float32)
            before = jnp.dot(pick, upper, preferred_element_type=jnp.float32) + offset
            slot = jnp.sum(before * pick, axis=0, keepdims=True).astype(jnp.int32)
            place = chosen * block + m * capacity + slot
            match = place == lanes
            hit = jnp.maximum(hit, match.astype(jnp.float32))
            place_col = jnp.transpose(place)
            weight_col = jnp.transpose(weights[k : k + 1, :])
            mixing = mixing + jnp.where(place_col == columns, weight_col, 0.0)
            offset = offset + jnp.sum(pick, axis=1, keepdims=True)
        rows = normed[m * tok_count : (m + 1) * tok_count, :]
        buffer = buffer + jnp.dot(hit.astype(jnp.bfloat16), rows, preferred_element_type=jnp.float32)
        mixing_ref[m] = mixing
    buffer_ref[...] = buffer.astype(jnp.bfloat16)


def prepare(inputs, gain, routes, weights, experts, capacity):
    micro, tok_count, width = inputs.shape
    slots = experts * micro * capacity
    return pl.pallas_call(
        lambda *refs: prepare_kernel(*refs, experts=experts, capacity=capacity),
        out_shape=(
            jax.ShapeDtypeStruct((slots, width), jnp.bfloat16),
            jax.ShapeDtypeStruct((micro, tok_count, slots), jnp.float32),
        ),
    )(
        inputs.reshape(micro * tok_count, width),
        gain.reshape(1, width),
        jnp.swapaxes(routes, 1, 2),
        jnp.swapaxes(weights, 1, 2),
    )


def body(tokens, routes, combine_weights, norm_gain, gate_up, down):
    inputs = tokens[0]
    micro, tok_count, width = inputs.shape
    experts = lax.axis_size("z")
    topk = routes.shape[3]
    capacity = 2 * ((3 * tok_count * topk + 4 * experts - 1) // (4 * experts))
    block = micro * capacity
    buffer, mixing = prepare(inputs, norm_gain[0], routes[0], combine_weights[0], experts, capacity)
    buffer = buffer.reshape(experts, block, width)
    incoming = lax.all_to_all(buffer, "z", split_axis=0, concat_axis=0, tiled=True)
    partner_rows = swap_cores(incoming)
    own = expert_half(incoming.reshape(-1, width), gate_up[0, 0], down[0, 0])
    lent = expert_half(partner_rows.reshape(-1, width), gate_up[0, 0], down[0, 0])
    other_half = swap_cores(lent.reshape(incoming.shape))
    results = (own.reshape(incoming.shape).astype(jnp.float32) + other_half.astype(jnp.float32))
    results = results.astype(jnp.bfloat16)
    returned = lax.all_to_all(results, "z", split_axis=0, concat_axis=0, tiled=True)
    table = returned.reshape(-1, width)
    combined = jnp.einsum(
        "mtq,qd->mtd",
        mixing,
        table.astype(jnp.float32),
        precision=lax.Precision.HIGH,
        preferred_element_type=jnp.float32,
    )
    mixed = inputs.astype(jnp.float32) + combined
    moved = from_behind(mixed.astype(jnp.bfloat16), "section", 1)
    return moved[None]


def solution(mesh):
    sections, spread = mesh.devices.shape
    chips = Mesh(mesh.devices.reshape(sections, spread // 2, 2), ("section", "z", "core"))
    split = ("z", "core")
    return jax.shard_map(
        body,
        mesh=chips,
        in_specs=(
            P("section", None, split, None),
            P("section", None, split, None),
            P("section", None, split, None),
            P("section", None),
            P("section", split, None, None),
            P("section", split, None, None),
        ),
        out_specs=P("section", None, split, None),
        check_vma=False,
    )
```
